1024 devices in a mesh: slab: 64 (over z, y), leaf: 16 (over x, core).
Axes of the slice: x: 8, y: 8, z: 8, core: 2. Of those that a mesh axis runs over, the one named last changes fastest.
Arguments:
- probes: bfloat16 [524288, 128], P(('slab', 'leaf')), may hold values from -6 to 6
- near_blocks: bfloat16 [1024, 3, 512, 512], P(('slab', 'leaf')), may hold values from -0.15625 to 0.15625
- near_offsets: int32 [1024, 3], P(('slab', 'leaf')), may hold values from -1 to 1
- far_basis: bfloat16 [10, 524288, 128], P(None, ('slab', 'leaf')), may hold values from -0.25 to 0.25
Outputs:
- product: float32 [524288, 128], P(('slab', 'leaf'))
The draws below stay inside these ranges and needn't reach their ends.
Inputs may be any that keep to these rules, and one draw needn't show every extreme that they name: `near_offsets`: offsets that point outside the leaves meet zero probes.
All inputs are finite; a program needn't handle non-finite values.
Results may differ from the reference program's by a relative error of at most 0.0025.
Values may be sent and summed in bfloat16 or wider, within the bound.
No kernel may reach another device: no remote copies, remote signals or barrier semaphores. Data moves between devices by JAX's collectives and lax.ppermute only.
A program may use at most 32 MiB of HBM per device.

```python
import jax
import jax.numpy as jnp
from jax import lax

POINTS_LEAF = 512
RANK = 128
NEAR = 3
PROBES = 128
LEAVES = 1024
POINTS = 524288
LEVELS = 10


def place_ends(entries, rng, low, high):
    longest = entries.shape.index(max(entries.shape))
    spots = []
    for shift in (0, 1):
        where = [jax.random.randint(jax.random.fold_in(rng, axis), (), 0, length) for axis, length in enumerate(entries.shape)]
        where[longest] = (where[longest] + shift) % entries.shape[longest]
        spots.append(tuple(where))
    return entries.at[spots[0]].set(low).at[spots[1]].set(high)


def block_levels(key, extent, pieces, smallest, top_value):
    gain, own = 1.0, jax.random.fold_in(key, 6)
    for axis_at, shards_of in pieces:
        draws = jnp.exp(jax.random.uniform(jax.random.fold_in(own, axis_at), (shards_of,), jnp.float32, smallest / len(pieces), top_value / len(pieces)))
        gain = gain * jnp.repeat(draws, extent[axis_at] // shards_of).reshape([-1 if axis == axis_at else 1 for axis in range(len(extent))])
    return gain


def noise(own_key, dims, scale, most, shards=(), kind=jnp.bfloat16):
    array = scale * jax.random.normal(own_key, dims, jnp.float32)
    if shards:
        array = array * block_levels(own_key, dims, shards, -0.22, 0.18)
    return jnp.clip(array, -most, most).astype(kind)


def setup_inputs(seed: int = 0) -> dict:
    keys = jax.random.split(jax.random.key(seed), 5)
    probes = noise(keys[0], (POINTS, PROBES), 1.0, 6.0, ((0, 1024),))
    near_blocks = noise(keys[1], (LEAVES, NEAR, POINTS_LEAF, POINTS_LEAF), (NEAR * POINTS_LEAF) ** -0.5, 0.15625, ((0, 1024),))
    near_offsets = place_ends(jax.random.randint(keys[2], (LEAVES, NEAR), -1, 2), jax.random.fold_in(keys[2], 1), -1, 1).astype(jnp.int32)
    far_basis = noise(keys[3], (LEVELS, POINTS, RANK), POINTS_LEAF ** -0.5, 0.25, ((1, 1024),))
    return {"probes": probes, "near_blocks": near_blocks, "near_offsets": near_offsets, "far_basis": far_basis}


def reference(probes, near_blocks, near_offsets, far_basis):
    leaves = near_blocks.shape[0]
    blocks = probes.reshape(leaves, POINTS_LEAF, PROBES)
    empty = jnp.zeros((1, POINTS_LEAF, PROBES), probes.dtype)
    padded = jnp.concatenate([empty, blocks, empty], axis=0)

    def near_leaf(packed_args):
        block_set, offset_row, leaf_index = packed_args
        near_sum = jnp.zeros((POINTS_LEAF, PROBES), jnp.float32)
        for member in range(NEAR):
            where_from = (leaf_index + offset_row[member] + 1).astype(jnp.int32)
            neighbour = lax.dynamic_index_in_dim(padded, where_from, 0, keepdims=False)
            near_sum = near_sum + jnp.dot(block_set[member], neighbour, preferred_element_type=jnp.float32)
        return near_sum

    output = lax.map(near_leaf, (near_blocks, near_offsets, jnp.arange(leaves, dtype=jnp.int32)))
    wide_probes = blocks.astype(jnp.float32)
    for level in range(LEVELS):
        level_basis = far_basis[level].reshape(leaves, POINTS_LEAF, RANK).astype(jnp.float32)
        projected = jnp.einsum("npr,npq->nrq", level_basis, wide_probes)
        nodes = leaves >> (level + 1)
        grouped = projected.reshape(nodes, 2, 2 ** level, RANK, PROBES).sum(axis=2)
        swapped = grouped[:, ::-1]
        sibling = jnp.broadcast_to(swapped[:, :, None], (nodes, 2, 2 ** level, RANK, PROBES)).reshape(leaves, RANK, PROBES)
        coupling = (sibling * (2.0 ** (-0.5 * level))).astype(jnp.bfloat16)
        output = output + jnp.einsum("npr,nrq->npq", level_basis, coupling.astype(jnp.float32))
    return output.reshape(leaves * POINTS_LEAF, PROBES)
```

```python
import jax
import jax.numpy as jnp
from jax import lax
from jax.sharding import PartitionSpec as P


def extended(block, sides, width):
    for axis, dim in sides:
        count = lax.axis_size(axis)
        forward = [(i, i + 1) for i in range(count - 1)]
        backward = [(target, source) for source, target in forward]
        low = lax.ppermute(
            lax.slice_in_dim(block, block.shape[dim] - width, None, axis=dim), axis, forward
        )
        high = lax.ppermute(lax.slice_in_dim(block, 0, width, axis=dim), axis, backward)
        block = jnp.concatenate([low, block, high], axis=dim)
    return block


def swapped(value, axis, bit):
    mask = 2**bit
    pairs = [(source, source ^ mask) for source in range(lax.axis_size(axis))]
    return lax.ppermute(value, axis, pairs)


def body(probes, near_blocks, near_offsets, far_basis):
    leaf_rows = probes.shape[0]
    levels = far_basis.shape[0]
    padded = extended(probes, ((("slab", "leaf"), 0),), leaf_rows)
    near_sum = jnp.zeros(probes.shape, jnp.float32)
    for member in range(near_blocks.shape[1]):
        window_start = (near_offsets[0, member] + 1) * leaf_rows
        window = lax.dynamic_slice_in_dim(padded, window_start, leaf_rows, 0)
        near_sum = near_sum + jnp.dot(
            near_blocks[0, member], window, preferred_element_type=jnp.float32
        )
    projected = jnp.einsum("lpr,pq->lrq", far_basis, probes, preferred_element_type=jnp.float32)
    rank, width = projected.shape[1], projected.shape[2]
    leaf_bits = lax.axis_size("leaf").bit_length() - 1
    slab_bits = levels - leaf_bits
    leaf_index = lax.axis_index("leaf")

    low = [projected[level] for level in range(leaf_bits)]
    upper = projected[leaf_bits:]
    sibling = [None] * levels
    for tree_bit in range(leaf_bits):
        half = upper.shape[1] // 2
        bit = (leaf_index >> tree_bit) & 1
        keep = lax.dynamic_slice_in_dim(upper, bit * half, half, axis=1)
        send = lax.dynamic_slice_in_dim(upper, (1 - bit) * half, half, axis=1)
        whole = leaf_bits - tree_bit
        packet = jnp.concatenate(
            [jnp.stack(low[tree_bit:]).reshape(-1, width), send.reshape(-1, width)], axis=0
        )
        incoming = swapped(packet, "leaf", tree_bit)
        incoming_low = incoming[: whole * rank].reshape(whole, rank, width)
        incoming_upper = incoming[whole * rank :].reshape(slab_bits, half, width)
        sibling[tree_bit] = incoming_low[0]
        for level in range(tree_bit + 1, leaf_bits):
            low[level] = low[level] + incoming_low[level - tree_bit]
        upper = keep + incoming_upper

    partial_sums = [upper[step] for step in range(slab_bits)]
    shares = []
    for step in range(slab_bits):
        incoming = swapped(jnp.stack(partial_sums[step:]), "slab", step)
        level = leaf_bits + step
        shares.append((incoming[0] * 2.0 ** (-0.5 * level)).astype(jnp.bfloat16))
        for later in range(step + 1, slab_bits):
            partial_sums[later] = partial_sums[later] + incoming[later - step]

    gathered = jnp.stack(shares)
    for tree_bit in reversed(range(leaf_bits)):
        bit = (leaf_index >> tree_bit) & 1
        other = swapped(gathered, "leaf", tree_bit)
        gathered = jnp.where(
            bit == 0,
            jnp.concatenate([gathered, other], axis=1),
            jnp.concatenate([other, gathered], axis=1),
        )

    output = near_sum
    for level in range(leaf_bits):
        coupling = (sibling[level] * 2.0 ** (-0.5 * level)).astype(jnp.bfloat16)
        output = output + jnp.dot(far_basis[level], coupling, preferred_element_type=jnp.float32)
    for step in range(slab_bits):
        output = output + jnp.dot(
            far_basis[leaf_bits + step], gathered[step], preferred_element_type=jnp.float32
        )
    return output


def solution(mesh):
    return jax.shard_map(
        body,
        mesh=mesh,
        in_specs=(
            P(("slab", "leaf"), None),
            P(("slab", "leaf"), None, None, None),
            P(("slab", "leaf"), None),
            P(None, ("slab", "leaf"), None),
        ),
        out_specs=P(("slab", "leaf"), None),
        check_vma=False,
    )
```

```python
import jax
import jax.numpy as jnp
from jax import lax
from jax.sharding import PartitionSpec as P


def extended(block, sides, width):
    for axis, dim in sides:
        count = lax.axis_size(axis)
        forward = [(i, i + 1) for i in range(count - 1)]
        backward = [(target, source) for source, target in forward]
        low = lax.ppermute(
            lax.slice_in_dim(block, block.shape[dim] - width, None, axis=dim), axis, forward
        )
        high = lax.ppermute(lax.slice_in_dim(block, 0, width, axis=dim), axis, backward)
        block = jnp.concatenate([low, block, high], axis=dim)
    return block


def body(probes, near_blocks, near_offsets, far_basis):
    leaf_rows = probes.shape[0]
    levels = far_basis.shape[0]
    padded = extended(probes, ((("slab", "leaf"), 0),), leaf_rows)
    near_sum = jnp.zeros(probes.shape, jnp.float32)
    for member in range(near_blocks.shape[1]):
        window_start = (near_offsets[0, member] + 1) * leaf_rows
        window = lax.dynamic_slice_in_dim(padded, window_start, leaf_rows, 0)
        near_sum = near_sum + jnp.dot(
            near_blocks[0, member], window, preferred_element_type=jnp.float32
        )
    projected = jnp.einsum("lpr,pq->lrq", far_basis, probes, preferred_element_type=jnp.float32)
    rank, width = projected.shape[1], projected.shape[2]
    leaves = lax.axis_size("leaf")
    slabs = lax.axis_size("slab")
    leaf_bits = leaves.bit_length() - 1
    slab_bits = levels - leaf_bits
    share = rank // leaves

    parts = lax.all_to_all(
        projected.reshape(levels, leaves, share, width), "leaf", 1, 1, tiled=True
    )
    couplings_low = []
    for level in range(leaf_bits):
        nodes = leaves >> (level + 1)
        grouped = parts[level].reshape(nodes, 2, 2**level, share, width).sum(axis=2)[:, ::-1]
        sibling = jnp.broadcast_to(
            grouped[:, :, None], (nodes, 2, 2**level, share, width)
        ).reshape(leaves, share, width)
        couplings_low.append((sibling * 2.0 ** (-0.5 * level)).astype(jnp.bfloat16))
    totals = parts[leaf_bits:].sum(axis=1)

    slab_index = lax.axis_index("slab")
    relative = jnp.arange(slabs, dtype=jnp.int32)
    distance = jnp.bitwise_xor(relative, slab_index)
    level_of = jnp.zeros_like(distance)
    for bit in range(1, slab_bits):
        level_of = level_of + (distance >= 2**bit).astype(jnp.int32)
    received = lax.all_to_all(jnp.take(totals, level_of, axis=0), "slab", 0, 0, tiled=True)
    by_distance = jnp.take(received, distance, axis=0)
    couplings_high = []
    for step in range(slab_bits):
        level = leaf_bits + step
        sibling = by_distance[2**step : 2 ** (step + 1)].sum(axis=0)
        couplings_high.append((sibling * 2.0 ** (-0.5 * level)).astype(jnp.bfloat16))

    outgoing = jnp.concatenate(
        [
            jnp.stack(couplings_low, axis=1),
            jnp.broadcast_to(jnp.stack(couplings_high)[None], (leaves, slab_bits, share, width)),
        ],
        axis=1,
    )
    coupling = lax.all_to_all(outgoing, "leaf", 0, 0, tiled=True)
    coupling = coupling.transpose(1, 0, 2, 3).reshape(levels, rank, width)
    output = near_sum + jnp.einsum(
        "lpr,lrq->pq", far_basis, coupling, preferred_element_type=jnp.float32
    )
    return output


def solution(mesh):
    return jax.shard_map(
        body,
        mesh=mesh,
        in_specs=(
            P(("slab", "leaf"), None),
            P(("slab", "leaf"), None, None, None),
            P(("slab", "leaf"), None),
            P(None, ("slab", "leaf"), None),
        ),
        out_specs=P(("slab", "leaf"), None),
        check_vma=False,
    )
```

```python
import jax
import jax.numpy as jnp
from jax import lax
from jax.sharding import PartitionSpec as P


def extended(block, sides, width):
    for axis, dim in sides:
        count = lax.axis_size(axis)
        forward = [(i, i + 1) for i in range(count - 1)]
        backward = [(target, source) for source, target in forward]
        low = lax.ppermute(
            lax.slice_in_dim(block, block.shape[dim] - width, None, axis=dim), axis, forward
        )
        high = lax.ppermute(lax.slice_in_dim(block, 0, width, axis=dim), axis, backward)
        block = jnp.concatenate([low, block, high], axis=dim)
    return block


def body(probes, near_blocks, near_offsets, far_basis):
    leaf_rows = probes.shape[0]
    levels = far_basis.shape[0]
    padded = extended(probes, ((("z", "y", "leaf"), 0),), leaf_rows)
    near_sum = jnp.zeros(probes.shape, jnp.float32)
    for member in range(near_blocks.shape[1]):
        window_start = (near_offsets[0, member] + 1) * leaf_rows
        window = lax.dynamic_slice_in_dim(padded, window_start, leaf_rows, 0)
        near_sum = near_sum + jnp.dot(
            near_blocks[0, member], window, preferred_element_type=jnp.float32
        )
    projected = jnp.einsum("lpr,pq->lrq", far_basis, probes, preferred_element_type=jnp.float32)
    rank, width = projected.shape[1], projected.shape[2]
    leaves = lax.axis_size("leaf")
    leaf_bits = leaves.bit_length() - 1
    slab_bits = levels - leaf_bits
    share = rank // leaves
    shares = projected.reshape(levels, leaves, share, width)

    parts = lax.all_to_all(shares, "leaf", 1, 1, tiled=True)
    couplings_low = []
    for level in range(leaf_bits):
        nodes = leaves >> (level + 1)
        grouped = parts[level].reshape(nodes, 2, 2**level, share, width).sum(axis=2)[:, ::-1]
        sibling = jnp.broadcast_to(
            grouped[:, :, None], (nodes, 2, 2**level, share, width)
        ).reshape(leaves, share, width)
        couplings_low.append((sibling * 2.0 ** (-0.5 * level)).astype(jnp.bfloat16))
    totals = parts[leaf_bits:].sum(axis=1)

    couplings_high = []
    pending = totals
    for axis in SLAB_AXES:
        members = lax.axis_size(axis)
        bits = members.bit_length() - 1
        index = lax.axis_index(axis)
        distance = jnp.bitwise_xor(jnp.arange(members, dtype=jnp.int32), index)
        level_of = jnp.zeros_like(distance)
        for bit in range(1, bits):
            level_of = level_of + (distance >= 2**bit).astype(jnp.int32)
        outgoing = jnp.take(pending[:bits], level_of, axis=0)[:, None]
        if pending.shape[0] > bits:
            rest = jnp.broadcast_to(
                pending[bits:][None], (members,) + pending[bits:].shape
            )
            outgoing = jnp.concatenate([outgoing, rest], axis=1)
        received = lax.all_to_all(outgoing, axis, 0, 0, tiled=True)
        for bit in range(bits):
            level = leaf_bits + len(couplings_high)
            begin = jnp.bitwise_xor(index >> bit, 1) << bit
            sibling = lax.dynamic_slice_in_dim(received[:, 0], begin, 2**bit, 0).sum(axis=0)
            couplings_high.append((sibling * 2.0 ** (-0.5 * level)).astype(jnp.bfloat16))
        pending = received[:, 1:].sum(axis=0)

    high = jnp.stack(couplings_high)
    outgoing = jnp.concatenate(
        [
            jnp.stack(couplings_low, axis=1),
            jnp.broadcast_to(high[None], (leaves,) + high.shape),
        ],
        axis=1,
    )
    coupling = lax.all_to_all(outgoing, "leaf", 0, 0, tiled=True)
    coupling = coupling.transpose(1, 0, 2, 3).reshape(levels, rank, width)
    output = near_sum + jnp.einsum(
        "lpr,lrq->pq", far_basis, coupling, preferred_element_type=jnp.float32
    )
    return output


SLAB_AXES = ("y", "z")


def solution(mesh):
    slabs, leaves = mesh.devices.shape
    inner = 2 ** ((slabs.bit_length() - 1) // 2)
    mesh = jax.sharding.Mesh(
        mesh.devices.reshape(slabs // inner, inner, leaves), ("z", "y", "leaf")
    )
    placed = ("z", "y", "leaf")
    return jax.shard_map(
        body,
        mesh=mesh,
        in_specs=(
            P(placed, None),
            P(placed, None, None, None),
            P(placed, None),
            P(None, placed, None),
        ),
        out_specs=P(placed, None),
        check_vma=False,
    )
```

```python
import jax
import jax.numpy as jnp
from jax import lax
from jax.sharding import PartitionSpec as P

PLACED = ("slab", "x", "core")


def extended(block, sides, width):
    for axis, dim in sides:
        count = lax.axis_size(axis)
        forward = [(i, i + 1) for i in range(count - 1)]
        backward = [(target, source) for source, target in forward]
        low = lax.ppermute(
            lax.slice_in_dim(block, block.shape[dim] - width, None, axis=dim), axis, forward
        )
        high = lax.ppermute(lax.slice_in_dim(block, 0, width, axis=dim), axis, backward)
        block = jnp.concatenate([low, block, high], axis=dim)
    return block


def body(probes, near_blocks, near_offsets, far_basis):
    leaf_rows = probes.shape[0]
    levels = far_basis.shape[0]
    padded = extended(probes, ((PLACED, 0),), leaf_rows)
    near_sum = jnp.zeros(probes.shape, jnp.float32)
    for member in range(near_blocks.shape[1]):
        window_start = (near_offsets[0, member] + 1) * leaf_rows
        window = lax.dynamic_slice_in_dim(padded, window_start, leaf_rows, 0)
        near_sum = near_sum + jnp.dot(
            near_blocks[0, member], window, preferred_element_type=jnp.float32
        )
    projected = jnp.einsum("lpr,pq->lrq", far_basis, probes, preferred_element_type=jnp.float32)
    rank, width = projected.shape[1], projected.shape[2]
    chips = lax.axis_size("x")
    slabs = lax.axis_size("slab")
    leaf_bits = chips.bit_length()
    slab_bits = levels - leaf_bits
    half = rank // 2
    share = half // chips
    core = lax.axis_index("core")
    swap = [(0, 1), (1, 0)]

    keep = lax.dynamic_slice_in_dim(projected[1:], core * half, half, axis=1)
    send = lax.dynamic_slice_in_dim(projected[1:], (1 - core) * half, half, axis=1)
    incoming = lax.ppermute(
        jnp.concatenate([projected[0], send.reshape(-1, width)], axis=0), "core", swap
    )
    coupling_first = (incoming[:rank] * 2.0**0).astype(jnp.bfloat16)
    paired = keep + incoming[rank:].reshape(levels - 1, half, width)

    parts = lax.all_to_all(
        paired.reshape(levels - 1, chips, share, width), "x", 1, 1, tiled=True
    )
    couplings_low = []
    for level in range(1, leaf_bits):
        sub = level - 1
        nodes = chips >> (sub + 1)
        grouped = parts[sub].reshape(nodes, 2, 2**sub, share, width).sum(axis=2)[:, ::-1]
        sibling = jnp.broadcast_to(
            grouped[:, :, None], (nodes, 2, 2**sub, share, width)
        ).reshape(chips, share, width)
        couplings_low.append((sibling * 2.0 ** (-0.5 * level)).astype(jnp.bfloat16))
    totals = parts[leaf_bits - 1 :].sum(axis=1)

    slab_index = lax.axis_index("slab")
    relative = jnp.arange(slabs, dtype=jnp.int32)
    distance = jnp.bitwise_xor(relative, slab_index)
    level_of = jnp.zeros_like(distance)
    for bit in range(1, slab_bits):
        level_of = level_of + (distance >= 2**bit).astype(jnp.int32)
    received = lax.all_to_all(jnp.take(totals, level_of, axis=0), "slab", 0, 0, tiled=True)
    by_distance = jnp.take(received, distance, axis=0)
    couplings_high = []
    for step in range(slab_bits):
        level = leaf_bits + step
        sibling = by_distance[2**step : 2 ** (step + 1)].sum(axis=0)
        couplings_high.append((sibling * 2.0 ** (-0.5 * level)).astype(jnp.bfloat16))

    high = jnp.stack(couplings_high)
    outgoing = jnp.concatenate(
        [
            jnp.stack(couplings_low, axis=1),
            jnp.broadcast_to(high[None], (chips,) + high.shape),
        ],
        axis=1,
    )
    returned = lax.all_to_all(outgoing, "x", 0, 0, tiled=True)
    mine = returned.transpose(1, 0, 2, 3).reshape(levels - 1, half, width)
    other = lax.ppermute(mine, "core", swap)
    coupling_rest = jnp.where(
        core == 0,
        jnp.concatenate([mine, other], axis=1),
        jnp.concatenate([other, mine], axis=1),
    )
    output = near_sum + jnp.dot(far_basis[0], coupling_first, preferred_element_type=jnp.float32)
    output = output + jnp.einsum(
        "lpr,lrq->pq", far_basis[1:], coupling_rest, preferred_element_type=jnp.float32
    )
    return output


def solution(mesh):
    slabs, leaves = mesh.devices.shape
    mesh = jax.sharding.Mesh(mesh.devices.reshape(slabs, leaves // 2, 2), PLACED)
    return jax.shard_map(
        body,
        mesh=mesh,
        in_specs=(
            P(PLACED, None),
            P(PLACED, None, None, None),
            P(PLACED, None),
            P(None, PLACED, None),
        ),
        out_specs=P(PLACED, None),
        check_vma=False,
    )
```

```python
import jax
import jax.numpy as jnp
from jax import lax
from jax.sharding import PartitionSpec as P

PLACED = ("slab", "x", "core")


def body(probes, near_blocks, near_offsets, far_basis):
    leaf_rows = probes.shape[0]
    levels = far_basis.shape[0]
    projected = jnp.einsum("lpr,pq->lrq", far_basis, probes, preferred_element_type=jnp.float32)
    rank, width = projected.shape[1], projected.shape[2]
    chips = lax.axis_size("x")
    slabs = lax.axis_size("slab")
    leaf_bits = chips.bit_length()
    slab_bits = levels - leaf_bits
    half = rank // 2
    share = half // chips
    core = lax.axis_index("core")
    swap = [(0, 1), (1, 0)]

    keep = lax.dynamic_slice_in_dim(projected[1:], core * half, half, axis=1)
    send = lax.dynamic_slice_in_dim(projected[1:], (1 - core) * half, half, axis=1)
    incoming = lax.ppermute(
        jnp.concatenate(
            [projected[0], send.reshape(-1, width), probes.astype(jnp.float32)], axis=0
        ),
        "core",
        swap,
    )
    coupling_first = (incoming[:rank] * 2.0**0).astype(jnp.bfloat16)
    paired = keep + incoming[rank : rank + (levels - 1) * half].reshape(levels - 1, half, width)

    partner = incoming[rank + (levels - 1) * half :].astype(probes.dtype)
    devices = slabs * chips * 2
    pairs = []
    for odd in range(1, devices - 1, 2):
        pairs += [(odd, odd + 1), (odd + 1, odd)]
    across = lax.ppermute(probes, PLACED, pairs)
    padded = jnp.concatenate(
        [
            jnp.where(core == 0, across, partner),
            probes,
            jnp.where(core == 0, partner, across),
        ],
        axis=0,
    )
    near_sum = jnp.zeros(probes.shape, jnp.float32)
    for member in range(near_blocks.shape[1]):
        window_start = (near_offsets[0, member] + 1) * leaf_rows
        window = lax.dynamic_slice_in_dim(padded, window_start, leaf_rows, 0)
        near_sum = near_sum + jnp.dot(
            near_blocks[0, member], window, preferred_element_type=jnp.float32
        )

    parts = lax.all_to_all(
        paired.reshape(levels - 1, chips, share, width), "x", 1, 1, tiled=True
    )
    couplings_low = []
    for level in range(1, leaf_bits):
        sub = level - 1
        nodes = chips >> (sub + 1)
        grouped = parts[sub].reshape(nodes, 2, 2**sub, share, width).sum(axis=2)[:, ::-1]
        sibling = jnp.broadcast_to(
            grouped[:, :, None], (nodes, 2, 2**sub, share, width)
        ).reshape(chips, share, width)
        couplings_low.append((sibling * 2.0 ** (-0.5 * level)).astype(jnp.bfloat16))
    totals = parts[leaf_bits - 1 :].sum(axis=1)

    slab_index = lax.axis_index("slab")
    relative = jnp.arange(slabs, dtype=jnp.int32)
    distance = jnp.bitwise_xor(relative, slab_index)
    level_of = jnp.zeros_like(distance)
    for bit in range(1, slab_bits):
        level_of = level_of + (distance >= 2**bit).astype(jnp.int32)
    received = lax.all_to_all(jnp.take(totals, level_of, axis=0), "slab", 0, 0, tiled=True)
    by_distance = jnp.take(received, distance, axis=0)
    couplings_high = []
    for step in range(slab_bits):
        level = leaf_bits + step
        sibling = by_distance[2**step : 2 ** (step + 1)].sum(axis=0)
        couplings_high.append((sibling * 2.0 ** (-0.5 * level)).astype(jnp.bfloat16))

    high = jnp.stack(couplings_high)
    outgoing = jnp.concatenate(
        [
            jnp.stack(couplings_low, axis=1),
            jnp.broadcast_to(high[None], (chips,) + high.shape),
        ],
        axis=1,
    )
    returned = lax.all_to_all(outgoing, "x", 0, 0, tiled=True)
    mine = returned.transpose(1, 0, 2, 3).reshape(levels - 1, half, width)
    other = lax.ppermute(mine, "core", swap)
    coupling_rest = jnp.where(
        core == 0,
        jnp.concatenate([mine, other], axis=1),
        jnp.concatenate([other, mine], axis=1),
    )
    output = near_sum + jnp.dot(far_basis[0], coupling_first, preferred_element_type=jnp.float32)
    output = output + jnp.einsum(
        "lpr,lrq->pq", far_basis[1:], coupling_rest, preferred_element_type=jnp.float32
    )
    return output


def solution(mesh):
    slabs, leaves = mesh.devices.shape
    mesh = jax.sharding.Mesh(mesh.devices.reshape(slabs, leaves // 2, 2), PLACED)
    return jax.shard_map(
        body,
        mesh=mesh,
        in_specs=(
            P(PLACED, None),
            P(PLACED, None, None, None),
            P(PLACED, None),
            P(None, PLACED, None),
        ),
        out_specs=P(PLACED, None),
        check_vma=False,
    )
```

```python
import jax
import jax.numpy as jnp
from jax import lax
from jax.sharding import PartitionSpec as P

PLACED = ("slab", "x", "core")


def body(probes, near_blocks, near_offsets, far_basis):
    leaf_rows = probes.shape[0]
    levels = far_basis.shape[0]
    projected = jnp.einsum("lpr,pq->lrq", far_basis, probes, preferred_element_type=jnp.float32)
    rank, width = projected.shape[1], projected.shape[2]
    chips = lax.axis_size("x")
    slabs = lax.axis_size("slab")
    leaf_bits = chips.bit_length()
    slab_bits = levels - leaf_bits
    half = rank // 2
    share = half // chips
    core = lax.axis_index("core")
    swap = [(0, 1), (1, 0)]

    keep = lax.dynamic_slice_in_dim(projected[1:], core * half, half, axis=1)
    send = lax.dynamic_slice_in_dim(projected[1:], (1 - core) * half, half, axis=1)
    incoming = lax.ppermute(
        jnp.concatenate(
            [projected[0], send.reshape(-1, width), probes.astype(jnp.float32)], axis=0
        ),
        "core",
        swap,
    )
    coupling_first = (incoming[:rank] * 2.0**0).astype(jnp.bfloat16)
    paired = keep + incoming[rank : rank + (levels - 1) * half].reshape(levels - 1, half, width)

    partner = incoming[rank + (levels - 1) * half :].astype(probes.dtype)
    devices = slabs * chips * 2
    pairs = []
    for odd in range(1, devices - 1, 2):
        pairs += [(odd, odd + 1), (odd + 1, odd)]
    across = lax.ppermute(probes, PLACED, pairs)
    padded = jnp.concatenate(
        [
            jnp.where(core == 0, across, partner),
            probes,
            jnp.where(core == 0, partner, across),
        ],
        axis=0,
    )
    near_sum = jnp.zeros(probes.shape, jnp.float32)
    for member in range(near_blocks.shape[1]):
        window_start = (near_offsets[0, member] + 1) * leaf_rows
        window = lax.dynamic_slice_in_dim(padded, window_start, leaf_rows, 0)
        near_sum = near_sum + jnp.dot(
            near_blocks[0, member], window, preferred_element_type=jnp.float32
        )

    parts = lax.all_to_all(
        paired.reshape(levels - 1, chips, share, width), "x", 1, 1, tiled=True
    )
    couplings_low = []
    for level in range(1, leaf_bits):
        sub = level - 1
        nodes = chips >> (sub + 1)
        grouped = parts[sub].reshape(nodes, 2, 2**sub, share, width).sum(axis=2)[:, ::-1]
        sibling = jnp.broadcast_to(
            grouped[:, :, None], (nodes, 2, 2**sub, share, width)
        ).reshape(chips, share, width)
        couplings_low.append((sibling * 2.0 ** (-0.5 * level)).astype(jnp.bfloat16))
    totals = parts[leaf_bits - 1 :].sum(axis=1)

    slab_index = lax.axis_index("slab")
    relative = jnp.arange(slabs, dtype=jnp.int32)
    distance = jnp.bitwise_xor(relative, slab_index)
    level_of = jnp.zeros_like(distance)
    for bit in range(1, slab_bits):
        level_of = level_of + (distance >= 2**bit).astype(jnp.int32)
    received = lax.all_to_all(jnp.take(totals, level_of, axis=0), "slab", 0, 0, tiled=True)
    by_distance = jnp.take(received, distance, axis=0)
    couplings_high = []
    for step in range(slab_bits):
        level = leaf_bits + step
        sibling = by_distance[2**step : 2 ** (step + 1)].sum(axis=0)
        couplings_high.append((sibling * 2.0 ** (-0.5 * level)).astype(jnp.bfloat16))

    high = jnp.stack(couplings_high)
    outgoing = jnp.concatenate(
        [
            jnp.stack(couplings_low, axis=1),
            jnp.broadcast_to(high[None], (chips,) + high.shape),
        ],
        axis=1,
    )
    everyone = jnp.broadcast_to(outgoing[:, None], (chips, 2) + outgoing.shape[1:])
    returned = lax.all_to_all(
        everyone.reshape((chips * 2,) + outgoing.shape[1:]), ("x", "core"), 0, 0, tiled=True
    )
    coupling_rest = (
        returned.reshape((chips, 2) + outgoing.shape[1:])
        .transpose(2, 1, 0, 3, 4)
        .reshape(levels - 1, rank, width)
    )
    output = near_sum + jnp.dot(far_basis[0], coupling_first, preferred_element_type=jnp.float32)
    output = output + jnp.einsum(
        "lpr,lrq->pq", far_basis[1:], coupling_rest, preferred_element_type=jnp.float32
    )
    return output


def solution(mesh):
    slabs, leaves = mesh.devices.shape
    mesh = jax.sharding.Mesh(mesh.devices.reshape(slabs, leaves // 2, 2), PLACED)
    return jax.shard_map(
        body,
        mesh=mesh,
        in_specs=(
            P(PLACED, None),
            P(PLACED, None, None, None),
            P(PLACED, None),
            P(None, PLACED, None),
        ),
        out_specs=P(PLACED, None),
        check_vma=False,
    )
```

```python
import jax
import jax.numpy as jnp
from jax import lax
from jax.sharding import PartitionSpec as P

PLACED = ("slab", "x", "core")


def body(probes, near_blocks, near_offsets, far_basis):
    leaf_rows = probes.shape[0]
    levels = far_basis.shape[0]
    projected = jnp.einsum("lpr,pq->lrq", far_basis, probes, preferred_element_type=jnp.float32)
    rank, width = projected.shape[1], projected.shape[2]
    chips = lax.axis_size("x")
    slabs = lax.axis_size("slab")
    leaf_bits = chips.bit_length()
    slab_bits = levels - leaf_bits
    half = rank // 2
    share = half // chips
    core = lax.axis_index("core")
    swap = [(0, 1), (1, 0)]

    keep = lax.dynamic_slice_in_dim(projected[1:], core * half, half, axis=1)
    send = lax.dynamic_slice_in_dim(projected[1:], (1 - core) * half, half, axis=1)
    incoming = lax.ppermute(
        jnp.concatenate([projected[0], send.reshape(-1, width)], axis=0), "core", swap
    )
    coupling_first = (incoming[:rank] * 2.0**0).astype(jnp.bfloat16)
    paired = keep + incoming[rank:].reshape(levels - 1, half, width)

    parts = lax.all_to_all(
        paired.reshape(levels - 1, chips, share, width), "x", 1, 1, tiled=True
    )
    couplings_low = []
    for level in range(1, leaf_bits):
        sub = level - 1
        nodes = chips >> (sub + 1)
        grouped = parts[sub].reshape(nodes, 2, 2**sub, share, width).sum(axis=2)[:, ::-1]
        sibling = jnp.broadcast_to(
            grouped[:, :, None], (nodes, 2, 2**sub, share, width)
        ).reshape(chips, share, width)
        couplings_low.append((sibling * 2.0 ** (-0.5 * level)).astype(jnp.bfloat16))
    totals = parts[leaf_bits - 1 :].sum(axis=1)

    slab_index = lax.axis_index("slab")
    relative = jnp.arange(slabs, dtype=jnp.int32)
    distance = jnp.bitwise_xor(relative, slab_index)
    level_of = jnp.zeros_like(distance)
    for bit in range(1, slab_bits):
        level_of = level_of + (distance >= 2**bit).astype(jnp.int32)
    received = lax.all_to_all(jnp.take(totals, level_of, axis=0), "slab", 0, 0, tiled=True)
    by_distance = jnp.take(received, distance, axis=0)
    couplings_high = []
    for step in range(slab_bits):
        level = leaf_bits + step
        sibling = by_distance[2**step : 2 ** (step + 1)].sum(axis=0)
        couplings_high.append((sibling * 2.0 ** (-0.5 * level)).astype(jnp.bfloat16))

    sent, _ = lax.optimization_barrier((probes, received))
    partner = lax.ppermute(sent, "core", swap)
    devices = slabs * chips * 2
    pairs = []
    for odd in range(1, devices - 1, 2):
        pairs += [(odd, odd + 1), (odd + 1, odd)]
    across = lax.ppermute(sent, PLACED, pairs)
    padded = jnp.concatenate(
        [
            jnp.where(core == 0, across, partner),
            probes,
            jnp.where(core == 0, partner, across),
        ],
        axis=0,
    )
    near_sum = jnp.zeros(probes.shape, jnp.float32)
    for member in range(near_blocks.shape[1]):
        window_start = (near_offsets[0, member] + 1) * leaf_rows
        window = lax.dynamic_slice_in_dim(padded, window_start, leaf_rows, 0)
        near_sum = near_sum + jnp.dot(
            near_blocks[0, member], window, preferred_element_type=jnp.float32
        )

    high = jnp.stack(couplings_high)
    outgoing = jnp.concatenate(
        [
            jnp.stack(couplings_low, axis=1),
            jnp.broadcast_to(high[None], (chips,) + high.shape),
        ],
        axis=1,
    )
    everyone = jnp.broadcast_to(outgoing[:, None], (chips, 2) + outgoing.shape[1:])
    returned = lax.all_to_all(
        everyone.reshape((chips * 2,) + outgoing.shape[1:]), ("x", "core"), 0, 0, tiled=True
    )
    far_rest = (
        far_basis[1:]
        .reshape(levels - 1, leaf_rows, 2, chips, share)
        .transpose(1, 3, 2, 0, 4)
        .reshape(leaf_rows, -1)
    )
    output = near_sum + jnp.dot(far_basis[0], coupling_first, preferred_element_type=jnp.float32)
    output = output + jnp.dot(
        far_rest, returned.reshape(-1, width), preferred_element_type=jnp.float32
    )
    return output


def solution(mesh):
    slabs, leaves = mesh.devices.shape
    mesh = jax.sharding.Mesh(mesh.devices.reshape(slabs, leaves // 2, 2), PLACED)
    return jax.shard_map(
        body,
        mesh=mesh,
        in_specs=(
            P(PLACED, None),
            P(PLACED, None, None, None),
            P(PLACED, None),
            P(None, PLACED, None),
        ),
        out_specs=P(PLACED, None),
        check_vma=False,
    )
```

```python
import jax
import jax.numpy as jnp
from jax import lax
from jax.sharding import PartitionSpec as P

PLACED = ("slab", "x", "core")


def body(probes, near_blocks, near_offsets, far_basis):
    leaf_rows = probes.shape[0]
    levels = far_basis.shape[0]
    projected = jnp.einsum("lpr,pq->lrq", far_basis, probes, preferred_element_type=jnp.float32)
    rank, width = projected.shape[1], projected.shape[2]
    chips = lax.axis_size("x")
    slabs = lax.axis_size("slab")
    leaf_bits = chips.bit_length()
    slab_bits = levels - leaf_bits
    half = rank // 2
    share = half // chips
    core = lax.axis_index("core")
    swap = [(0, 1), (1, 0)]

    keep = lax.dynamic_slice_in_dim(projected[1:], core * half, half, axis=1)
    send = lax.dynamic_slice_in_dim(projected[1:], (1 - core) * half, half, axis=1)
    incoming = lax.ppermute(
        jnp.concatenate(
            [projected[0], send.reshape(-1, width), probes.astype(jnp.float32)], axis=0
        ),
        "core",
        swap,
    )
    coupling_first = (incoming[:rank] * 2.0**0).astype(jnp.bfloat16)
    paired = keep + incoming[rank : rank + (levels - 1) * half].reshape(levels - 1, half, width)

    partner = incoming[rank + (levels - 1) * half :].astype(probes.dtype)
    devices = slabs * chips * 2
    pairs = []
    for odd in range(1, devices - 1, 2):
        pairs += [(odd, odd + 1), (odd + 1, odd)]
    across = lax.ppermute(probes, PLACED, pairs)
    padded = jnp.concatenate(
        [
            jnp.where(core == 0, across, partner),
            probes,
            jnp.where(core == 0, partner, across),
        ],
        axis=0,
    )
    near_sum = jnp.zeros(probes.shape, jnp.float32)
    for member in range(near_blocks.shape[1]):
        window_start = (near_offsets[0, member] + 1) * leaf_rows
        window = lax.dynamic_slice_in_dim(padded, window_start, leaf_rows, 0)
        near_sum = near_sum + jnp.dot(
            near_blocks[0, member], window, preferred_element_type=jnp.float32
        )

    parts = lax.all_to_all(
        paired.reshape(levels - 1, chips, share, width), "x", 1, 1, tiled=True
    )
    couplings_low = []
    for level in range(1, leaf_bits):
        sub = level - 1
        nodes = chips >> (sub + 1)
        grouped = parts[sub].reshape(nodes, 2, 2**sub, share, width).sum(axis=2)[:, ::-1]
        sibling = jnp.broadcast_to(
            grouped[:, :, None], (nodes, 2, 2**sub, share, width)
        ).reshape(chips, share, width)
        couplings_low.append((sibling * 2.0 ** (-0.5 * level)).astype(jnp.bfloat16))
    totals = parts[leaf_bits - 1 :].sum(axis=1)

    slab_index = lax.axis_index("slab")
    relative = jnp.arange(slabs, dtype=jnp.int32)
    distance = jnp.bitwise_xor(relative, slab_index)
    level_of = jnp.zeros_like(distance)
    for bit in range(1, slab_bits):
        level_of = level_of + (distance >= 2**bit).astype(jnp.int32)
    received = lax.all_to_all(jnp.take(totals, level_of, axis=0), "slab", 0, 0, tiled=True)
    by_distance = jnp.take(received, distance, axis=0)
    couplings_high = []
    for step in range(slab_bits):
        level = leaf_bits + step
        sibling = by_distance[2**step : 2 ** (step + 1)].sum(axis=0)
        couplings_high.append((sibling * 2.0 ** (-0.5 * level)).astype(jnp.bfloat16))

    high = jnp.stack(couplings_high)
    outgoing = jnp.concatenate(
        [
            jnp.stack(couplings_low, axis=1),
            jnp.broadcast_to(high[None], (chips,) + high.shape),
        ],
        axis=1,
    )
    everyone = jnp.broadcast_to(outgoing[:, None], (chips, 2) + outgoing.shape[1:])
    returned = lax.all_to_all(
        everyone.reshape((chips * 2,) + outgoing.shape[1:]), ("x", "core"), 0, 0, tiled=True
    )
    far_rest = (
        far_basis[1:]
        .reshape(levels - 1, leaf_rows, 2, chips, share)
        .transpose(1, 3, 2, 0, 4)
        .reshape(leaf_rows, -1)
    )
    output = near_sum + jnp.dot(far_basis[0], coupling_first, preferred_element_type=jnp.float32)
    output = output + jnp.dot(
        far_rest, returned.reshape(-1, width), preferred_element_type=jnp.float32
    )
    return output


def solution(mesh):
    slabs, leaves = mesh.devices.shape
    mesh = jax.sharding.Mesh(mesh.devices.reshape(slabs, leaves // 2, 2), PLACED)
    return jax.shard_map(
        body,
        mesh=mesh,
        in_specs=(
            P(PLACED, None),
            P(PLACED, None, None, None),
            P(PLACED, None),
            P(None, PLACED, None),
        ),
        out_specs=P(PLACED, None),
        check_vma=False,
    )
```

```python
import jax
import jax.numpy as jnp
from jax import lax
from jax.sharding import PartitionSpec as P

PLACED = ("slab", "x", "core")


def body(probes, near_blocks, near_offsets, far_basis):
    leaf_rows = probes.shape[0]
    levels = far_basis.shape[0]
    projected = jnp.einsum("lpr,pq->lrq", far_basis, probes, preferred_element_type=jnp.float32)
    rank, width = projected.shape[1], projected.shape[2]
    chips = lax.axis_size("x")
    slabs = lax.axis_size("slab")
    leaf_bits = chips.bit_length()
    slab_bits = levels - leaf_bits
    half = rank // 2
    share = half // chips
    core = lax.axis_index("core")
    swap = [(0, 1), (1, 0)]

    keep = lax.dynamic_slice_in_dim(projected[1:], core * half, half, axis=1)
    send = lax.dynamic_slice_in_dim(projected[1:], (1 - core) * half, half, axis=1)
    incoming = lax.ppermute(
        jnp.concatenate(
            [projected[0], send.reshape(-1, width), probes.astype(jnp.float32)], axis=0
        ),
        "core",
        swap,
    )
    coupling_first = (incoming[:rank] * 2.0**0).astype(jnp.bfloat16)
    paired = keep + incoming[rank : rank + (levels - 1) * half].reshape(levels - 1, half, width)

    partner = incoming[rank + (levels - 1) * half :].astype(probes.dtype)
    devices = slabs * chips * 2
    pairs = []
    for odd in range(1, devices - 1, 2):
        pairs += [(odd, odd + 1), (odd + 1, odd)]
    across = lax.ppermute(probes, PLACED, pairs)
    padded = jnp.concatenate(
        [
            jnp.where(core == 0, across, partner),
            probes,
            jnp.where(core == 0, partner, across),
        ],
        axis=0,
    )
    near_sum = jnp.zeros(probes.shape, jnp.float32)
    for member in range(near_blocks.shape[1]):
        window_start = (near_offsets[0, member] + 1) * leaf_rows
        window = lax.dynamic_slice_in_dim(padded, window_start, leaf_rows, 0)
        near_sum = near_sum + jnp.dot(
            near_blocks[0, member], window, preferred_element_type=jnp.float32
        )

    parts = lax.all_to_all(
        paired.reshape(levels - 1, chips, share, width), "x", 1, 1, tiled=True
    )
    couplings_low = []
    for level in range(1, leaf_bits):
        sub = level - 1
        nodes = chips >> (sub + 1)
        grouped = parts[sub].reshape(nodes, 2, 2**sub, share, width).sum(axis=2)[:, ::-1]
        sibling = jnp.broadcast_to(
            grouped[:, :, None], (nodes, 2, 2**sub, share, width)
        ).reshape(chips, share, width)
        couplings_low.append((sibling * 2.0 ** (-0.5 * level)).astype(jnp.bfloat16))
    totals = parts[leaf_bits - 1 :].sum(axis=1)

    slab_index = lax.axis_index("slab")
    outgoing = jnp.zeros((slabs,) + totals.shape[1:], totals.dtype)
    starts = []
    for step in range(slab_bits):
        begin = jnp.bitwise_xor(slab_index >> step, 1) << step
        starts.append(begin)
        run = jnp.broadcast_to(totals[step][None], (2**step,) + totals.shape[1:])
        outgoing = lax.dynamic_update_slice_in_dim(outgoing, run, begin, 0)
    received = lax.all_to_all(outgoing, "slab", 0, 0, tiled=True)
    couplings_high = []
    for step in range(slab_bits):
        level = leaf_bits + step
        sibling = lax.dynamic_slice_in_dim(received, starts[step], 2**step, 0).sum(axis=0)
        couplings_high.append((sibling * 2.0 ** (-0.5 * level)).astype(jnp.bfloat16))

    high = jnp.stack(couplings_high)
    outgoing = jnp.concatenate(
        [
            jnp.stack(couplings_low, axis=1),
            jnp.broadcast_to(high[None], (chips,) + high.shape),
        ],
        axis=1,
    )
    everyone = jnp.broadcast_to(outgoing[:, None], (chips, 2) + outgoing.shape[1:])
    returned = lax.all_to_all(
        everyone.reshape((chips * 2,) + outgoing.shape[1:]), ("x", "core"), 0, 0, tiled=True
    )
    far_rest = (
        far_basis[1:]
        .reshape(levels - 1, leaf_rows, 2, chips, share)
        .transpose(1, 3, 2, 0, 4)
        .reshape(leaf_rows, -1)
    )
    output = near_sum + jnp.dot(far_basis[0], coupling_first, preferred_element_type=jnp.float32)
    output = output + jnp.dot(
        far_rest, returned.reshape(-1, width), preferred_element_type=jnp.float32
    )
    return output


def solution(mesh):
    slabs, leaves = mesh.devices.shape
    mesh = jax.sharding.Mesh(mesh.devices.reshape(slabs, leaves // 2, 2), PLACED)
    return jax.shard_map(
        body,
        mesh=mesh,
        in_specs=(
            P(PLACED, None),
            P(PLACED, None, None, None),
            P(PLACED, None),
            P(None, PLACED, None),
        ),
        out_specs=P(PLACED, None),
        check_vma=False,
    )
```

```python
import jax
import jax.numpy as jnp
from jax import lax
from jax.sharding import PartitionSpec as P

PLACED = ("slab", "x", "core")


def body(probes, near_blocks, near_offsets, far_basis):
    leaf_rows = probes.shape[0]
    levels = far_basis.shape[0]
    projected = jnp.einsum("lpr,pq->lrq", far_basis, probes, preferred_element_type=jnp.float32)
    rank, width = projected.shape[1], projected.shape[2]
    chips = lax.axis_size("x")
    slabs = lax.axis_size("slab")
    leaf_bits = chips.bit_length()
    slab_bits = levels - leaf_bits
    half = rank // 2
    share = half // chips
    core = lax.axis_index("core")
    swap = [(0, 1), (1, 0)]

    keep = lax.dynamic_slice_in_dim(projected[1:], core * half, half, axis=1)
    send = lax.dynamic_slice_in_dim(projected[1:], (1 - core) * half, half, axis=1)
    incoming = lax.ppermute(
        jnp.concatenate(
            [projected[0], send.reshape(-1, width), probes.astype(jnp.float32)], axis=0
        ),
        "core",
        swap,
    )
    coupling_first = (incoming[:rank] * 2.0**0).astype(jnp.bfloat16)
    paired = keep + incoming[rank : rank + (levels - 1) * half].reshape(levels - 1, half, width)

    partner = incoming[rank + (levels - 1) * half :].astype(probes.dtype)
    devices = slabs * chips * 2
    pairs = []
    for odd in range(1, devices - 1, 2):
        pairs += [(odd, odd + 1), (odd + 1, odd)]
    across = lax.ppermute(probes, PLACED, pairs)
    padded = jnp.concatenate(
        [
            jnp.where(core == 0, across, partner),
            probes,
            jnp.where(core == 0, partner, across),
        ],
        axis=0,
    )
    near_sum = jnp.zeros(probes.shape, jnp.float32)
    for member in range(near_blocks.shape[1]):
        window_start = (near_offsets[0, member] + 1) * leaf_rows
        window = lax.dynamic_slice_in_dim(padded, window_start, leaf_rows, 0)
        near_sum = near_sum + jnp.dot(
            near_blocks[0, member], window, preferred_element_type=jnp.float32
        )

    parts = lax.all_to_all(
        paired.reshape(levels - 1, chips, share, width), "x", 1, 1, tiled=True
    )
    couplings_low = []
    for level in range(1, leaf_bits):
        sub = level - 1
        nodes = chips >> (sub + 1)
        grouped = parts[sub].reshape(nodes, 2, 2**sub, share, width).sum(axis=2)[:, ::-1]
        sibling = jnp.broadcast_to(
            grouped[:, :, None], (nodes, 2, 2**sub, share, width)
        ).reshape(chips, share, width)
        couplings_low.append((sibling * 2.0 ** (-0.5 * level)).astype(jnp.bfloat16))
    totals = parts[leaf_bits - 1 :].sum(axis=1)

    slab_index = lax.axis_index("slab")
    distance = jnp.bitwise_xor(jnp.arange(slabs, dtype=jnp.int32), slab_index)
    outgoing = jnp.broadcast_to(totals[0][None], (slabs,) + totals.shape[1:])
    starts = []
    for step in range(slab_bits):
        starts.append(jnp.bitwise_xor(slab_index >> step, 1) << step)
        if step:
            outgoing = jnp.where(
                (distance >= 2**step)[:, None, None], totals[step][None], outgoing
            )
    received = lax.all_to_all(outgoing, "slab", 0, 0, tiled=True)
    couplings_high = []
    for step in range(slab_bits):
        level = leaf_bits + step
        sibling = lax.dynamic_slice_in_dim(received, starts[step], 2**step, 0).sum(axis=0)
        couplings_high.append((sibling * 2.0 ** (-0.5 * level)).astype(jnp.bfloat16))

    high = jnp.stack(couplings_high)
    outgoing = jnp.concatenate(
        [
            jnp.stack(couplings_low, axis=1),
            jnp.broadcast_to(high[None], (chips,) + high.shape),
        ],
        axis=1,
    )
    everyone = jnp.broadcast_to(outgoing[:, None], (chips, 2) + outgoing.shape[1:])
    returned = lax.all_to_all(
        everyone.reshape((chips * 2,) + outgoing.shape[1:]), ("x", "core"), 0, 0, tiled=True
    )
    far_rest = (
        far_basis[1:]
        .reshape(levels - 1, leaf_rows, 2, chips, share)
        .transpose(1, 3, 2, 0, 4)
        .reshape(leaf_rows, -1)
    )
    output = near_sum + jnp.dot(far_basis[0], coupling_first, preferred_element_type=jnp.float32)
    output = output + jnp.dot(
        far_rest, returned.reshape(-1, width), preferred_element_type=jnp.float32
    )
    return output


def solution(mesh):
    slabs, leaves = mesh.devices.shape
    mesh = jax.sharding.Mesh(mesh.devices.reshape(slabs, leaves // 2, 2), PLACED)
    return jax.shard_map(
        body,
        mesh=mesh,
        in_specs=(
            P(PLACED, None),
            P(PLACED, None, None, None),
            P(PLACED, None),
            P(None, PLACED, None),
        ),
        out_specs=P(PLACED, None),
        check_vma=False,
    )
```

```python
import jax
import jax.numpy as jnp
from jax import lax
from jax.sharding import PartitionSpec as P

PLACED = ("slab", "x", "core")


def body(probes, near_blocks, near_offsets, far_basis):
    leaf_rows = probes.shape[0]
    levels = far_basis.shape[0]
    projected = jnp.einsum("lpr,pq->lrq", far_basis, probes, preferred_element_type=jnp.float32)
    rank, width = projected.shape[1], projected.shape[2]
    chips = lax.axis_size("x")
    slabs = lax.axis_size("slab")
    leaf_bits = chips.bit_length()
    slab_bits = levels - leaf_bits
    half = rank // 2
    share = half // chips
    core = lax.axis_index("core")
    swap = [(0, 1), (1, 0)]

    keep = lax.dynamic_slice_in_dim(projected[1:], core * half, half, axis=1)
    send = lax.dynamic_slice_in_dim(projected[1:], (1 - core) * half, half, axis=1)
    incoming = lax.ppermute(
        jnp.concatenate(
            [projected[0], send.reshape(-1, width), probes.astype(jnp.float32)], axis=0
        ),
        "core",
        swap,
    )
    coupling_first = (incoming[:rank] * 2.0**0).astype(jnp.bfloat16)
    paired = keep + incoming[rank : rank + (levels - 1) * half].reshape(levels - 1, half, width)

    partner = incoming[rank + (levels - 1) * half :].astype(probes.dtype)
    devices = slabs * chips * 2
    pairs = []
    for odd in range(1, devices - 1, 2):
        pairs += [(odd, odd + 1), (odd + 1, odd)]
    across = lax.ppermute(probes, PLACED, pairs)
    padded = jnp.concatenate(
        [
            jnp.where(core == 0, across, partner),
            probes,
            jnp.where(core == 0, partner, across),
        ],
        axis=0,
    )
    near_sum = jnp.zeros(probes.shape, jnp.float32)
    for member in range(near_blocks.shape[1]):
        window_start = (near_offsets[0, member] + 1) * leaf_rows
        window = lax.dynamic_slice_in_dim(padded, window_start, leaf_rows, 0)
        near_sum = near_sum + jnp.dot(
            near_blocks[0, member], window, preferred_element_type=jnp.float32
        )

    parts = lax.all_to_all(
        paired.reshape(levels - 1, chips, share, width), "x", 1, 1, tiled=True
    )
    couplings_low = []
    for level in range(1, leaf_bits):
        sub = level - 1
        nodes = chips >> (sub + 1)
        grouped = parts[sub].reshape(nodes, 2, 2**sub, share, width).sum(axis=2)[:, ::-1]
        sibling = jnp.broadcast_to(
            grouped[:, :, None], (nodes, 2, 2**sub, share, width)
        ).reshape(chips, share, width)
        couplings_low.append((sibling * 2.0 ** (-0.5 * level)).astype(jnp.bfloat16))
    totals = parts[leaf_bits - 1 :].sum(axis=1)

    slab_index = lax.axis_index("slab")
    distance = jnp.bitwise_xor(jnp.arange(slabs, dtype=jnp.int32), slab_index)
    outgoing = jnp.broadcast_to(totals[0][None], (slabs,) + totals.shape[1:])
    starts = []
    for step in range(slab_bits):
        starts.append(jnp.bitwise_xor(slab_index >> step, 1) << step)
        if step:
            outgoing = jnp.where(
                (distance >= 2**step)[:, None, None], totals[step][None], outgoing
            )
    received = lax.all_to_all(outgoing, "slab", 0, 0, tiled=True)
    couplings_high = []
    for step in range(slab_bits):
        level = leaf_bits + step
        sibling = lax.dynamic_slice_in_dim(received, starts[step], 2**step, 0).sum(axis=0)
        couplings_high.append((sibling * 2.0 ** (-0.5 * level)).astype(jnp.bfloat16))

    high = jnp.stack(couplings_high)
    outgoing = jnp.concatenate(
        [
            jnp.stack(couplings_low, axis=1),
            jnp.broadcast_to(high[None], (chips,) + high.shape),
        ],
        axis=1,
    )
    everyone = jnp.broadcast_to(outgoing[:, None], (chips, 2) + outgoing.shape[1:])
    returned = lax.all_to_all(
        everyone.reshape((chips * 2,) + outgoing.shape[1:]), ("x", "core"), 0, 0, tiled=True
    )
    far_rest = (
        far_basis[1:]
        .reshape(levels - 1, leaf_rows, 2, chips, share)
        .transpose(1, 3, 2, 0, 4)
        .reshape(leaf_rows, -1)
    )
    far_all = jnp.concatenate([far_basis[0], far_rest], axis=1)
    coupling_all = jnp.concatenate([coupling_first, returned.reshape(-1, width)], axis=0)
    output = near_sum + jnp.dot(far_all, coupling_all, preferred_element_type=jnp.float32)
    return output


def solution(mesh):
    slabs, leaves = mesh.devices.shape
    mesh = jax.sharding.Mesh(mesh.devices.reshape(slabs, leaves // 2, 2), PLACED)
    return jax.shard_map(
        body,
        mesh=mesh,
        in_specs=(
            P(PLACED, None),
            P(PLACED, None, None, None),
            P(PLACED, None),
            P(None, PLACED, None),
        ),
        out_specs=P(PLACED, None),
        check_vma=False,
    )
```

```python
import jax
import jax.numpy as jnp
from jax import lax
from jax.sharding import PartitionSpec as P

PLACED = ("slab", "x", "core")


def body(probes, near_blocks, near_offsets, far_basis):
    leaf_rows = probes.shape[0]
    levels = far_basis.shape[0]
    projected = jnp.einsum("lpr,pq->lrq", far_basis, probes, preferred_element_type=jnp.float32)
    rank, width = projected.shape[1], projected.shape[2]
    chips = lax.axis_size("x")
    slabs = lax.axis_size("slab")
    leaf_bits = chips.bit_length()
    slab_bits = levels - leaf_bits
    half = rank // 2
    share = half // chips
    core = lax.axis_index("core")
    swap = [(0, 1), (1, 0)]

    keep = lax.dynamic_slice_in_dim(projected[1:], core * half, half, axis=1)
    send = lax.dynamic_slice_in_dim(projected[1:], (1 - core) * half, half, axis=1)
    incoming = lax.ppermute(
        jnp.concatenate(
            [projected[0], send.reshape(-1, width), probes.astype(jnp.float32)], axis=0
        ),
        "core",
        swap,
    )
    coupling_first = (incoming[:rank] * 2.0**0).astype(jnp.bfloat16)
    paired = keep + incoming[rank : rank + (levels - 1) * half].reshape(levels - 1, half, width)

    partner = incoming[rank + (levels - 1) * half :].astype(probes.dtype)
    devices = slabs * chips * 2
    pairs = []
    for odd in range(1, devices - 1, 2):
        pairs += [(odd, odd + 1), (odd + 1, odd)]
    across = lax.ppermute(probes, PLACED, pairs)
    padded = jnp.concatenate(
        [
            jnp.where(core == 0, across, partner),
            probes,
            jnp.where(core == 0, partner, across),
        ],
        axis=0,
    )
    near_sum = jnp.zeros(probes.shape, jnp.float32)
    for member in range(near_blocks.shape[1]):
        window_start = (near_offsets[0, member] + 1) * leaf_rows
        window = lax.dynamic_slice_in_dim(padded, window_start, leaf_rows, 0)
        near_sum = near_sum + jnp.dot(
            near_blocks[0, member], window, preferred_element_type=jnp.float32
        )

    parts = lax.all_to_all(
        paired.reshape(levels - 1, chips, share, width), "x", 1, 1, tiled=True
    )
    couplings_low = []
    for level in range(1, leaf_bits):
        sub = level - 1
        nodes = chips >> (sub + 1)
        grouped = parts[sub].reshape(nodes, 2, 2**sub, share, width).sum(axis=2)[:, ::-1]
        sibling = jnp.broadcast_to(
            grouped[:, :, None], (nodes, 2, 2**sub, share, width)
        ).reshape(chips, share, width)
        couplings_low.append((sibling * 2.0 ** (-0.5 * level)).astype(jnp.bfloat16))
    totals = parts[leaf_bits - 1 :].sum(axis=1)

    slab_index = lax.axis_index("slab")
    distance = jnp.bitwise_xor(jnp.arange(slabs, dtype=jnp.int32), slab_index)
    outgoing = jnp.broadcast_to(totals[0][None], (slabs,) + totals.shape[1:])
    starts = []
    for step in range(slab_bits):
        starts.append(jnp.bitwise_xor(slab_index >> step, 1) << step)
        if step:
            outgoing = jnp.where(
                (distance >= 2**step)[:, None, None], totals[step][None], outgoing
            )
    received = lax.all_to_all(outgoing, "slab", 0, 0, tiled=True)
    couplings_high = []
    for step in range(slab_bits):
        level = leaf_bits + step
        sibling = lax.dynamic_slice_in_dim(received, starts[step], 2**step, 0).sum(axis=0)
        couplings_high.append((sibling * 2.0 ** (-0.5 * level)).astype(jnp.bfloat16))

    low = jnp.stack(couplings_low, axis=1)
    high = jnp.stack(couplings_high)
    everyone = jnp.concatenate(
        [
            jnp.broadcast_to(low[:, None], (chips, 2) + low.shape[1:]),
            jnp.broadcast_to(high[None, None], (chips, 2) + high.shape),
        ],
        axis=2,
    )
    returned = lax.all_to_all(
        everyone.reshape((chips * 2,) + everyone.shape[2:]), ("x", "core"), 0, 0, tiled=True
    )
    far_rest = (
        far_basis[1:]
        .reshape(levels - 1, leaf_rows, 2, chips, share)
        .transpose(1, 3, 2, 0, 4)
        .reshape(leaf_rows, -1)
    )
    far_all = jnp.concatenate([far_basis[0], far_rest], axis=1)
    coupling_all = jnp.concatenate([coupling_first, returned.reshape(-1, width)], axis=0)
    output = near_sum + jnp.dot(far_all, coupling_all, preferred_element_type=jnp.float32)
    return output


def solution(mesh):
    slabs, leaves = mesh.devices.shape
    mesh = jax.sharding.Mesh(mesh.devices.reshape(slabs, leaves // 2, 2), PLACED)
    return jax.shard_map(
        body,
        mesh=mesh,
        in_specs=(
            P(PLACED, None),
            P(PLACED, None, None, None),
            P(PLACED, None),
            P(None, PLACED, None),
        ),
        out_specs=P(PLACED, None),
        check_vma=False,
    )
```

```python
import jax
import jax.numpy as jnp
from jax import lax
from jax.sharding import PartitionSpec as P

PLACED = ("slab", "x", "core")


def body(probes, near_blocks, near_offsets, far_basis):
    leaf_rows = probes.shape[0]
    levels = far_basis.shape[0]
    projected = jnp.einsum("lpr,pq->lrq", far_basis, probes, preferred_element_type=jnp.float32)
    rank, width = projected.shape[1], projected.shape[2]
    chips = lax.axis_size("x")
    slabs = lax.axis_size("slab")
    leaf_bits = chips.bit_length()
    slab_bits = levels - leaf_bits
    half = rank // 2
    share = half // chips
    core = lax.axis_index("core")
    swap = [(0, 1), (1, 0)]

    keep = lax.dynamic_slice_in_dim(projected[1:], core * half, half, axis=1)
    send = lax.dynamic_slice_in_dim(projected[1:], (1 - core) * half, half, axis=1)
    incoming = lax.ppermute(
        jnp.concatenate(
            [projected[0], send.reshape(-1, width), probes.astype(jnp.float32)], axis=0
        ),
        "core",
        swap,
    )
    coupling_first = (incoming[:rank] * 2.0**0).astype(jnp.bfloat16)
    paired = keep + incoming[rank : rank + (levels - 1) * half].reshape(levels - 1, half, width)

    partner = incoming[rank + (levels - 1) * half :].astype(probes.dtype)
    devices = slabs * chips * 2
    pairs = []
    for odd in range(1, devices - 1, 2):
        pairs += [(odd, odd + 1), (odd + 1, odd)]
    across = lax.ppermute(probes, PLACED, pairs)
    padded = jnp.concatenate(
        [
            jnp.where(core == 0, across, partner),
            probes,
            jnp.where(core == 0, partner, across),
        ],
        axis=0,
    )
    near_sum = jnp.zeros(probes.shape, jnp.float32)
    for member in range(near_blocks.shape[1]):
        window_start = (near_offsets[0, member] + 1) * leaf_rows
        window = lax.dynamic_slice_in_dim(padded, window_start, leaf_rows, 0)
        near_sum = near_sum + jnp.dot(
            near_blocks[0, member], window, preferred_element_type=jnp.float32
        )

    parts = lax.all_to_all(
        paired.reshape(levels - 1, chips, share, width), "x", 1, 1, tiled=True
    )
    couplings_low = []
    for level in range(1, leaf_bits):
        sub = level - 1
        nodes = chips >> (sub + 1)
        grouped = parts[sub].reshape(nodes, 2, 2**sub, share, width).sum(axis=2)[:, ::-1]
        sibling = jnp.broadcast_to(
            grouped[:, :, None], (nodes, 2, 2**sub, share, width)
        ).reshape(chips, share, width)
        couplings_low.append((sibling * 2.0 ** (-0.5 * level)).astype(jnp.bfloat16))

    slab_index = lax.axis_index("slab")
    distance = jnp.bitwise_xor(jnp.arange(slabs, dtype=jnp.int32), slab_index)
    upper = parts[leaf_bits - 1 :]
    outgoing = jnp.broadcast_to(upper[0][None], (slabs,) + upper.shape[1:])
    starts = []
    for step in range(slab_bits):
        starts.append(jnp.bitwise_xor(slab_index >> step, 1) << step)
        if step:
            outgoing = jnp.where(
                (distance >= 2**step)[:, None, None, None], upper[step][None], outgoing
            )
    outgoing = outgoing.sum(axis=1)
    received = lax.all_to_all(outgoing, "slab", 0, 0, tiled=True)
    couplings_high = []
    for step in range(slab_bits):
        level = leaf_bits + step
        sibling = lax.dynamic_slice_in_dim(received, starts[step], 2**step, 0).sum(axis=0)
        couplings_high.append((sibling * 2.0 ** (-0.5 * level)).astype(jnp.bfloat16))

    low = jnp.stack(couplings_low, axis=1)
    high = jnp.stack(couplings_high)
    everyone = jnp.concatenate(
        [
            jnp.broadcast_to(low[:, None], (chips, 2) + low.shape[1:]),
            jnp.broadcast_to(high[None, None], (chips, 2) + high.shape),
        ],
        axis=2,
    )
    returned = lax.all_to_all(
        everyone.reshape((chips * 2,) + everyone.shape[2:]), ("x", "core"), 0, 0, tiled=True
    )
    far_rest = (
        far_basis[1:]
        .reshape(levels - 1, leaf_rows, 2, chips, share)
        .transpose(1, 3, 2, 0, 4)
        .reshape(leaf_rows, -1)
    )
    far_all = jnp.concatenate([far_basis[0], far_rest], axis=1)
    coupling_all = jnp.concatenate([coupling_first, returned.reshape(-1, width)], axis=0)
    output = near_sum + jnp.dot(far_all, coupling_all, preferred_element_type=jnp.float32)
    return output


def solution(mesh):
    slabs, leaves = mesh.devices.shape
    mesh = jax.sharding.Mesh(mesh.devices.reshape(slabs, leaves // 2, 2), PLACED)
    return jax.shard_map(
        body,
        mesh=mesh,
        in_specs=(
            P(PLACED, None),
            P(PLACED, None, None, None),
            P(PLACED, None),
            P(None, PLACED, None),
        ),
        out_specs=P(PLACED, None),
        check_vma=False,
    )
```
